1024 devices in a mesh: tile: 64 (over y_lo, z), kern: 16 (over x, y_hi, core).
Axes of the slice: x: 4, y: 8 (y_hi: 2, y_lo: 4; y = y_hi * 4 + y_lo), z: 16, core: 2. Of those that a mesh axis runs over, the one named last changes fastest.
Arguments:
- mask: bfloat16 [64, 128, 128], P('tile'), may hold values from 0 to 1
- kernels: bfloat16 [2, 16, 65, 65], P(None, 'kern'), may hold values from -0.09375 to 0.09375
- weights: float32 [16], P('kern'), may hold values from 0.03 to 0.1
- target: bfloat16 [64, 128, 128], P('tile'), may hold values from 0 to 1
- neighbours: int32 [64, 8], P('tile'), may hold values from -1 to 63, as said below
Outputs:
- gradient: float32 [64, 128, 128], P('tile', 'kern')
- resist: float32 [64, 128, 128], P('tile', 'kern')
The draws below stay inside these ranges and needn't reach their ends.
Inputs may be any that keep to these rules, and one draw needn't show every extreme that they name: `neighbours`: tile t lies alone in row t of a grid of 2 cells a row, in its last cell; an entry names the tile in the cell at that direction (north is the row before), or is -1 where that cell is empty or off the grid.
All inputs are finite; a program needn't handle non-finite values.
Results may differ from the reference program's by a relative error of at most 0.0017.
Values may be sent and summed in bfloat16 or wider, within the bound.
No kernel may reach another device: no remote copies, remote signals or barrier semaphores. Data moves between devices by JAX's collectives and lax.ppermute only.
A program may use at most 128 MiB of HBM per device.

```python
import math
import jax
import jax.numpy as jnp
from jax import lax

TILE = 128
KTAP = 65
KERNELS = 16
TILES_DEV = 1
TILES = 64


def draw_neighbours(key, part):
    row_count = TILES // TILES_DEV
    col_count = 2 * TILES_DEV
    row_keys = jax.random.split(key, row_count)

    def pick_columns(row_key):
        others = jax.random.permutation(row_key, col_count - 1)[:TILES_DEV - 1]
        return jnp.sort(jnp.concatenate([others, jnp.full((1,), col_count - 1, others.dtype)]))
    columns = jax.vmap(pick_columns)(row_keys)
    row_of = jnp.repeat(jnp.arange(row_count, dtype=jnp.int32), TILES_DEV)
    col_of = columns.reshape(-1).astype(jnp.int32)
    grid_table = jnp.full((row_count + 2, col_count + 2), -1, jnp.int32)
    grid_table = grid_table.at[row_of + 1, col_of + 1].set(jnp.arange(TILES, dtype=jnp.int32))
    row_steps = jnp.array([-1, -1, -1, 0, 0, 1, 1, 1], jnp.int32)
    col_steps = jnp.array([-1, 0, 1, -1, 1, -1, 0, 1], jnp.int32)
    return grid_table[row_of[:, None] + 1 + row_steps[None, :], col_of[:, None] + 1 + col_steps[None, :]]


def block_levels(key, dims, shards, smallest, high):
    def one(position, shards_of):
        steps = jax.random.uniform(jax.random.fold_in(jax.random.fold_in(key, 6), position), (shards_of,), jnp.float32, smallest / len(shards), high / len(shards))
        return jnp.repeat(jnp.exp(steps), dims[position] // shards_of).reshape((-1,) + (1,) * (len(dims) - position - 1))

    gain = one(*shards[0])
    for cut in shards[1:]:
        gain = gain * one(*cut)
    return gain


def centred(own_key, dims, width, bound, cuts=(), held_as=jnp.bfloat16):
    entries = width * jax.random.normal(own_key, dims, jnp.float32)
    if cuts:
        entries = entries * block_levels(own_key, dims, cuts, -0.22, 0.18)
    return jnp.clip(entries, -bound, bound).astype(held_as)


def setup_inputs(seed: int = 0) -> dict:
    streams_of = jax.random.split(jax.random.key(seed), 6)
    mask = jnp.clip(1.0 * jax.random.uniform(streams_of[0], (TILES, TILE, TILE), jnp.float32) ** block_levels(streams_of[0], (TILES, TILE, TILE), ((0, 64),), -0.2, 0.2), 0.0, 1.0).astype(jnp.bfloat16)
    kernels = centred(streams_of[1], (2, KERNELS, KTAP, KTAP), (KTAP * KTAP) ** -0.5, 0.09375, ((1, 16),))
    weights = jnp.clip(jnp.exp(math.log(0.1) - 1.2039728 * jax.random.uniform(streams_of[2], (KERNELS,), jnp.float32) ** block_levels(streams_of[2], (KERNELS,), ((0, 16),), -0.2, 0.2)), 0.03, 0.1)
    target = jnp.clip(1.0 * jax.random.uniform(streams_of[3], (TILES, TILE, TILE), jnp.float32) ** block_levels(streams_of[3], (TILES, TILE, TILE), ((0, 64),), -0.2, 0.2), 0.0, 1.0).astype(jnp.bfloat16)
    neighbours = draw_neighbours(jax.random.fold_in(streams_of[5], 71), 0)
    return {"mask": mask, "kernels": kernels, "weights": weights, "target": target, "neighbours": neighbours}


steepness = 8.0
threshold = 0.5


def extend(tiles, neighbours, half_width):
    tile_count = tiles.shape[0]
    tile_side = tiles.shape[-1]
    padded = jnp.concatenate([tiles, jnp.zeros_like(tiles[:1])], axis=0)
    chosen = jnp.where(neighbours < 0, tile_count, neighbours).astype(jnp.int32)
    beside_all = padded[chosen]
    cut_at = tile_side - half_width
    upper_band = jnp.concatenate([beside_all[:, 0, :, cut_at:, cut_at:], beside_all[:, 1, :, cut_at:, :], beside_all[:, 2, :, cut_at:, :half_width]], axis=3)
    middle_band = jnp.concatenate([beside_all[:, 3, :, :, cut_at:], tiles, beside_all[:, 4, :, :, :half_width]], axis=3)
    lower_band = jnp.concatenate([beside_all[:, 5, :, :half_width, cut_at:], beside_all[:, 6, :, :half_width, :], beside_all[:, 7, :, :half_width, :half_width]], axis=3)
    return jnp.concatenate([upper_band, middle_band, lower_band], axis=2)


def reference(mask, kernels, weights, target, neighbours):
    half_width = (KTAP - 1) // 2
    span = TILE + 4 * half_width
    offset = 2 * half_width
    grid_shape = (span, span)

    def crop(values):
        return values[..., offset:offset + TILE, offset:offset + TILE]

    extended = extend(mask.astype(jnp.float32)[:, None], neighbours, half_width)[:, 0]
    mask_spec = jnp.fft.rfft2(extended, s=grid_shape)
    real_taps = kernels[0].astype(jnp.float32)
    imag_taps = kernels[1].astype(jnp.float32)

    def fields_of(real_tap, imag_tap):
        real_spec = jnp.fft.rfft2(real_tap[::-1, ::-1], s=grid_shape)
        imag_spec = jnp.fft.rfft2(imag_tap[::-1, ::-1], s=grid_shape)
        field_re = crop(jnp.fft.irfft2(mask_spec * real_spec, s=grid_shape))
        field_im = crop(jnp.fft.irfft2(mask_spec * imag_spec, s=grid_shape))
        return field_re, field_im

    def add_intensity(total, inputs):
        real_tap, imag_tap, weight = inputs
        field_re, field_im = fields_of(real_tap, imag_tap)
        return total + weight * (field_re * field_re + field_im * field_im), None

    intensity, _ = lax.scan(add_intensity, jnp.zeros((TILES, TILE, TILE), jnp.float32), (real_taps, imag_taps, weights))
    resist = jax.nn.sigmoid(steepness * (intensity - threshold))
    sensitivity = 2.0 * (resist - target.astype(jnp.float32)) * steepness * resist * (1.0 - resist)

    def add_gradient(total, inputs):
        real_tap, imag_tap, weight = inputs
        field_re, field_im = fields_of(real_tap, imag_tap)
        scaled = 2.0 * weight * sensitivity
        source = jnp.stack([scaled * field_re, scaled * field_im], axis=1).astype(jnp.bfloat16)
        source_ext = extend(source, neighbours, half_width).astype(jnp.float32)
        source_spec = jnp.fft.rfft2(source_ext, s=grid_shape)
        combined = source_spec[:, 0] * jnp.fft.rfft2(real_tap, s=grid_shape) + source_spec[:, 1] * jnp.fft.rfft2(imag_tap, s=grid_shape)
        return total + crop(jnp.fft.irfft2(combined, s=grid_shape)), None

    gradient, _ = lax.scan(add_gradient, jnp.zeros((TILES, TILE, TILE), jnp.float32), (real_taps, imag_taps, weights))
    return gradient, resist
```

```python
import jax
import jax.numpy as jnp
from jax import lax
from jax.sharding import PartitionSpec as P

steepness = 8.0
threshold = 0.5


def padded_2(shard, sides, width):
    for axis, dim in sides:
        devices, length = (lax.axis_size(axis), shard.shape[dim])
        up = [(i, (i + 1) % devices) for i in range(devices - 1)]
        down = [(j, i) for i, j in up]
        last = lax.slice_in_dim(shard, length - width, length, axis=dim)
        first = lax.slice_in_dim(shard, 0, width, axis=dim)
        before = lax.ppermute(last, axis, up)
        after = lax.ppermute(first, axis, down)
        shard = jnp.concatenate([before, shard, after], axis=dim)
    return shard


def select_rows(source, chosen):
    tile_count = source.shape[0]
    picked = jnp.take(source, chosen % tile_count, axis=0)
    present = (chosen >= 0).astype(source.dtype)
    return picked * present[:, None, None, None]


def assemble(own_tiles, north_rows, south_rows, neighbours):
    half_width = north_rows.shape[2]
    tile_side = own_tiles.shape[3]
    cut_at = tile_side - half_width

    def beside_all(source, column):
        return select_rows(source, neighbours[:, column])

    upper_band = jnp.concatenate(
        [
            beside_all(north_rows, 0)[..., cut_at:],
            beside_all(north_rows, 1),
            beside_all(north_rows, 2)[..., :half_width],
        ],
        axis=3,
    )
    middle_band = jnp.concatenate(
        [
            beside_all(own_tiles, 3)[..., cut_at:],
            own_tiles,
            beside_all(own_tiles, 4)[..., :half_width],
        ],
        axis=3,
    )
    lower_band = jnp.concatenate(
        [
            beside_all(south_rows, 5)[..., cut_at:],
            beside_all(south_rows, 6),
            beside_all(south_rows, 7)[..., :half_width],
        ],
        axis=3,
    )
    return jnp.concatenate([upper_band, middle_band, lower_band], axis=2)


def group_size(tap_count):
    for candidate in range(min(tap_count, 16), 0, -1):
        if tap_count % candidate == 0:
            return candidate
    return 1


def banded(taps, width_in, width_out):
    tap_count = taps.shape[2]
    shape = (tap_count, width_out, width_in)
    along = lax.broadcasted_iota(jnp.int32, shape, 0)
    row = lax.broadcasted_iota(jnp.int32, shape, 1)
    col = lax.broadcasted_iota(jnp.int32, shape, 2)
    select = (col - row == along).astype(taps.dtype)
    band = jnp.einsum(
        "acb,bji->acji", taps.transpose(1, 0, 2), select, preferred_element_type=jnp.float32
    )
    return band.astype(taps.dtype)


def butterfly_sum(value, axis):
    devices = lax.axis_size(axis)
    bit = 1
    while bit < devices:
        pairs = [(i, i ^ bit) for i in range(devices)]
        value = value + lax.ppermute(value, axis, pairs)
        bit *= 2
    return value


def halving_scatter(value, axis, dim):
    devices = lax.axis_size(axis)
    place = lax.axis_index(axis)
    bit = devices // 2
    while bit >= 1:
        half = value.shape[dim] // 2
        upper = (place // bit) % 2
        keep = lax.dynamic_slice_in_dim(value, upper * half, half, dim)
        give = lax.dynamic_slice_in_dim(value, (1 - upper) * half, half, dim)
        pairs = [(i, i ^ bit) for i in range(devices)]
        value = keep + lax.ppermute(give, axis, pairs)
        bit //= 2
    return value


def correlate_forward(images, band, rows_out):
    tap_count = band.shape[0]
    group = group_size(tap_count)
    total = None
    for first in range(0, tap_count, group):
        stacked = jnp.stack(
            [images[:, first + step : first + step + rows_out, :] for step in range(group)], axis=1
        )
        term = lax.dot_general(
            stacked,
            band[first : first + group],
            (((1, 3), (0, 3)), ((), ())),
            preferred_element_type=jnp.float32,
        )
        total = term if total is None else total + term
    return total.transpose(0, 2, 1, 3)


def correlate_adjoint(images, band, rows_out):
    tap_count = band.shape[0]
    group = group_size(tap_count)
    total = None
    for first in range(0, tap_count, group):
        stacked = jnp.stack(
            [images[:, :, first + step : first + step + rows_out, :] for step in range(group)],
            axis=1,
        )
        term = lax.dot_general(
            stacked,
            band[first : first + group],
            (((1, 2, 4), (0, 1, 3)), ((), ())),
            preferred_element_type=jnp.float32,
        )
        total = term if total is None else total + term
    return total


def shards(mask, kernels, weights, target, neighbours):
    tile_side = mask.shape[1]
    local_kernels = kernels.shape[1]
    tap_count = kernels.shape[2]
    half_width = (tap_count - 1) // 2
    kern_count = lax.axis_size("kern")
    kern_place = lax.axis_index("kern")
    share_rows = tile_side // kern_count
    width_in = tile_side + 2 * half_width
    strips = jnp.stack([mask[:, :half_width, :], mask[:, tile_side - half_width :, :]])
    framed = padded_2(strips, (("tile", 0),), 1)
    north_rows = framed[0]
    south_rows = framed[3]
    extended = assemble(mask[:, None], north_rows[:, None], south_rows[:, None], neighbours)[:, 0]
    taps = kernels.reshape(2 * local_kernels, tap_count, tap_count)
    forward_band = banded(taps, width_in, tile_side)
    fields = correlate_forward(extended, forward_band, tile_side)
    doubled = jnp.concatenate([weights, weights])
    partial_sum = jnp.sum(doubled[None, :, None, None] * fields * fields, axis=1)
    intensity = butterfly_sum(partial_sum, "kern")
    resist_full = jax.nn.sigmoid(steepness * (intensity - threshold))
    sensitivity = (
        2.0
        * (resist_full - target.astype(jnp.float32))
        * steepness
        * resist_full
        * (1.0 - resist_full)
    )
    resist = lax.dynamic_slice_in_dim(resist_full, kern_place * share_rows, share_rows, 1)
    scaled = (2.0 * doubled)[None, :, None, None] * sensitivity[:, None] * fields
    adjoint_source = scaled.astype(jnp.bfloat16)
    source_strips = jnp.stack(
        [adjoint_source[:, :, :half_width, :], adjoint_source[:, :, tile_side - half_width :, :]]
    )
    source_framed = padded_2(source_strips, (("tile", 0),), 1)
    source_ext = assemble(adjoint_source, source_framed[0], source_framed[3], neighbours)
    adjoint_band = banded(taps[:, ::-1, ::-1], width_in, tile_side)
    gradient_term = correlate_adjoint(source_ext, adjoint_band, tile_side)
    gradient = halving_scatter(gradient_term, "kern", 1)
    return (gradient, resist)


def solution(mesh):
    in_specs = (
        P("tile", None, None),
        P(None, "kern", None, None),
        P("kern"),
        P("tile", None, None),
        P("tile", None),
    )
    out_specs = (P("tile", "kern", None), P("tile", "kern", None))
    return jax.shard_map(shards, mesh=mesh, in_specs=in_specs, out_specs=out_specs, check_vma=False)
```

```python
import jax
import jax.numpy as jnp
from jax import lax
from jax.sharding import PartitionSpec as P

steepness = 8.0
threshold = 0.5


def padded_2(shard, sides, width):
    for axis, dim in sides:
        devices, length = (lax.axis_size(axis), shard.shape[dim])
        up = [(i, (i + 1) % devices) for i in range(devices - 1)]
        down = [(j, i) for i, j in up]
        last = lax.slice_in_dim(shard, length - width, length, axis=dim)
        first = lax.slice_in_dim(shard, 0, width, axis=dim)
        before = lax.ppermute(last, axis, up)
        after = lax.ppermute(first, axis, down)
        shard = jnp.concatenate([before, shard, after], axis=dim)
    return shard


def select_rows(source, chosen):
    tile_count = source.shape[0]
    picked = jnp.take(source, chosen % tile_count, axis=0)
    present = (chosen >= 0).astype(source.dtype)
    return picked * present[:, None, None, None]


def assemble(own_tiles, north_rows, south_rows, neighbours):
    half_width = north_rows.shape[2]
    tile_side = own_tiles.shape[3]
    cut_at = tile_side - half_width

    def beside_all(source, column):
        return select_rows(source, neighbours[:, column])

    upper_band = jnp.concatenate(
        [
            beside_all(north_rows, 0)[..., cut_at:],
            beside_all(north_rows, 1),
            beside_all(north_rows, 2)[..., :half_width],
        ],
        axis=3,
    )
    middle_band = jnp.concatenate(
        [
            beside_all(own_tiles, 3)[..., cut_at:],
            own_tiles,
            beside_all(own_tiles, 4)[..., :half_width],
        ],
        axis=3,
    )
    lower_band = jnp.concatenate(
        [
            beside_all(south_rows, 5)[..., cut_at:],
            beside_all(south_rows, 6),
            beside_all(south_rows, 7)[..., :half_width],
        ],
        axis=3,
    )
    return jnp.concatenate([upper_band, middle_band, lower_band], axis=2)


def group_size(tap_count):
    for candidate in range(min(tap_count, 16), 0, -1):
        if tap_count % candidate == 0:
            return candidate
    return 1


def banded(taps, width_in, width_out):
    tap_count = taps.shape[2]
    shape = (tap_count, width_out, width_in)
    along = lax.broadcasted_iota(jnp.int32, shape, 0)
    row = lax.broadcasted_iota(jnp.int32, shape, 1)
    col = lax.broadcasted_iota(jnp.int32, shape, 2)
    select = (col - row == along).astype(taps.dtype)
    band = jnp.einsum(
        "acb,bji->acji", taps.transpose(1, 0, 2), select, preferred_element_type=jnp.float32
    )
    return band.astype(taps.dtype)


def scatter_sum(value, axis, dim):
    pieces = lax.all_to_all(value, axis, dim, 0, tiled=True)
    return jnp.sum(pieces, axis=0, keepdims=True)


def gather_blocks(block, axis, dim):
    devices = lax.axis_size(axis)
    copies = jnp.broadcast_to(block, (devices,) + block.shape[1:])
    pieces = lax.all_to_all(copies, axis, 0, 0, tiled=True)
    return jnp.concatenate(jnp.split(pieces, devices, axis=0), axis=dim)


def correlate_forward(images, band, rows_out):
    tap_count = band.shape[0]
    group = group_size(tap_count)
    total = None
    for first in range(0, tap_count, group):
        stacked = jnp.stack(
            [images[:, first + step : first + step + rows_out, :] for step in range(group)], axis=1
        )
        term = lax.dot_general(
            stacked,
            band[first : first + group],
            (((1, 3), (0, 3)), ((), ())),
            preferred_element_type=jnp.float32,
        )
        total = term if total is None else total + term
    return total.transpose(0, 2, 1, 3)


def correlate_adjoint(images, band, rows_out):
    tap_count = band.shape[0]
    group = group_size(tap_count)
    total = None
    for first in range(0, tap_count, group):
        stacked = jnp.stack(
            [images[:, :, first + step : first + step + rows_out, :] for step in range(group)],
            axis=1,
        )
        term = lax.dot_general(
            stacked,
            band[first : first + group],
            (((1, 2, 4), (0, 1, 3)), ((), ())),
            preferred_element_type=jnp.float32,
        )
        total = term if total is None else total + term
    return total


def shards(mask, kernels, weights, target, neighbours):
    tile_side = mask.shape[1]
    local_kernels = kernels.shape[1]
    tap_count = kernels.shape[2]
    half_width = (tap_count - 1) // 2
    kern_count = lax.axis_size("kern")
    kern_place = lax.axis_index("kern")
    share_rows = tile_side // kern_count
    width_in = tile_side + 2 * half_width
    strips = jnp.stack([mask[:, :half_width, :], mask[:, tile_side - half_width :, :]])
    framed = padded_2(strips, (("tile", 0),), 1)
    north_rows = framed[0]
    south_rows = framed[3]
    extended = assemble(mask[:, None], north_rows[:, None], south_rows[:, None], neighbours)[:, 0]
    taps = kernels.reshape(2 * local_kernels, tap_count, tap_count)
    forward_band = banded(taps, width_in, tile_side)
    fields = correlate_forward(extended, forward_band, tile_side)
    doubled = jnp.concatenate([weights, weights])
    partial_sum = jnp.sum(doubled[None, :, None, None] * fields * fields, axis=1)
    intensity = scatter_sum(partial_sum, "kern", 1)
    resist = jax.nn.sigmoid(steepness * (intensity - threshold))
    own_target = lax.dynamic_slice_in_dim(target, kern_place * share_rows, share_rows, 1)
    own_sensitivity = (
        2.0 * (resist - own_target.astype(jnp.float32)) * steepness * resist * (1.0 - resist)
    )
    sensitivity = gather_blocks(own_sensitivity, "kern", 1)
    scaled = (2.0 * doubled)[None, :, None, None] * sensitivity[:, None] * fields
    adjoint_source = scaled.astype(jnp.bfloat16)
    source_strips = jnp.stack(
        [adjoint_source[:, :, :half_width, :], adjoint_source[:, :, tile_side - half_width :, :]]
    )
    source_framed = padded_2(source_strips, (("tile", 0),), 1)
    source_ext = assemble(adjoint_source, source_framed[0], source_framed[3], neighbours)
    adjoint_band = banded(taps[:, ::-1, ::-1], width_in, tile_side)
    gradient_term = correlate_adjoint(source_ext, adjoint_band, tile_side)
    gradient = scatter_sum(gradient_term, "kern", 1)
    return (gradient, resist)


def solution(mesh):
    in_specs = (
        P("tile", None, None),
        P(None, "kern", None, None),
        P("kern"),
        P("tile", None, None),
        P("tile", None),
    )
    out_specs = (P("tile", "kern", None), P("tile", "kern", None))
    return jax.shard_map(shards, mesh=mesh, in_specs=in_specs, out_specs=out_specs, check_vma=False)
```

```python
import jax
import jax.numpy as jnp
from jax import lax
from jax.sharding import PartitionSpec as P

steepness = 8.0
threshold = 0.5


def padded_2(shard, sides, width):
    for axis, dim in sides:
        devices, length = (lax.axis_size(axis), shard.shape[dim])
        up = [(i, (i + 1) % devices) for i in range(devices - 1)]
        down = [(j, i) for i, j in up]
        last = lax.slice_in_dim(shard, length - width, length, axis=dim)
        first = lax.slice_in_dim(shard, 0, width, axis=dim)
        before = lax.ppermute(last, axis, up)
        after = lax.ppermute(first, axis, down)
        shard = jnp.concatenate([before, shard, after], axis=dim)
    return shard


def select_rows(source, chosen):
    tile_count = source.shape[0]
    picked = jnp.take(source, chosen % tile_count, axis=0)
    present = (chosen >= 0).astype(source.dtype)
    return picked * present[:, None, None, None]


def assemble(own_tiles, north_rows, south_rows, neighbours):
    half_width = north_rows.shape[2]
    tile_side = own_tiles.shape[3]
    cut_at = tile_side - half_width

    def beside_all(source, column):
        return select_rows(source, neighbours[:, column])

    upper_band = jnp.concatenate(
        [
            beside_all(north_rows, 0)[..., cut_at:],
            beside_all(north_rows, 1),
            beside_all(north_rows, 2)[..., :half_width],
        ],
        axis=3,
    )
    middle_band = jnp.concatenate(
        [
            beside_all(own_tiles, 3)[..., cut_at:],
            own_tiles,
            beside_all(own_tiles, 4)[..., :half_width],
        ],
        axis=3,
    )
    lower_band = jnp.concatenate(
        [
            beside_all(south_rows, 5)[..., cut_at:],
            beside_all(south_rows, 6),
            beside_all(south_rows, 7)[..., :half_width],
        ],
        axis=3,
    )
    return jnp.concatenate([upper_band, middle_band, lower_band], axis=2)


def banded(taps, width_in, width_out):
    tap_count = taps.shape[2]
    shape = (tap_count, width_out, width_in)
    along = lax.broadcasted_iota(jnp.int32, shape, 0)
    row = lax.broadcasted_iota(jnp.int32, shape, 1)
    col = lax.broadcasted_iota(jnp.int32, shape, 2)
    select = (col - row == along).astype(taps.dtype)
    band = jnp.einsum(
        "acb,bji->acji", taps.transpose(1, 0, 2), select, preferred_element_type=jnp.float32
    )
    return band.astype(taps.dtype)


def scatter_sum(value, axis, dim):
    pieces = lax.all_to_all(value, axis, dim, 0, tiled=True)
    return jnp.sum(pieces, axis=0, keepdims=True)


def gather_blocks(block, axis, dim):
    devices = lax.axis_size(axis)
    copies = jnp.broadcast_to(block, (devices,) + block.shape[1:])
    pieces = lax.all_to_all(copies, axis, 0, 0, tiled=True)
    return jnp.concatenate(jnp.split(pieces, devices, axis=0), axis=dim)


def shifted_rows(images, tap_count, rows_out):
    rows_in = images.shape[-2]
    shape = (tap_count, rows_out, rows_in)
    along = lax.broadcasted_iota(jnp.int32, shape, 0)
    row = lax.broadcasted_iota(jnp.int32, shape, 1)
    source = lax.broadcasted_iota(jnp.int32, shape, 2)
    return (source - row == along).astype(images.dtype)


def correlate_forward(images, band, rows_out):
    select = shifted_rows(images, band.shape[0], rows_out)
    stacked = jnp.einsum(
        "apr,tri->tapi", select, images, preferred_element_type=jnp.float32
    ).astype(images.dtype)
    total = jnp.einsum("tapi,acqi->tcpq", stacked, band, preferred_element_type=jnp.float32)
    return total


def correlate_adjoint(images, band, rows_out):
    select = shifted_rows(images, band.shape[0], rows_out)
    stacked = jnp.einsum(
        "apr,tcri->tacpi", select, images, preferred_element_type=jnp.float32
    ).astype(images.dtype)
    return jnp.einsum("tacpi,acqi->tpq", stacked, band, preferred_element_type=jnp.float32)


def shards(mask, kernels, weights, target, neighbours):
    tile_side = mask.shape[1]
    local_kernels = kernels.shape[1]
    tap_count = kernels.shape[2]
    half_width = (tap_count - 1) // 2
    kern_count = lax.axis_size("kern")
    kern_place = lax.axis_index("kern")
    share_rows = tile_side // kern_count
    width_in = tile_side + 2 * half_width
    strips = jnp.stack([mask[:, :half_width, :], mask[:, tile_side - half_width :, :]])
    framed = padded_2(strips, (("tile", 0),), 1)
    north_rows = framed[0]
    south_rows = framed[3]
    extended = assemble(mask[:, None], north_rows[:, None], south_rows[:, None], neighbours)[:, 0]
    taps = kernels.reshape(2 * local_kernels, tap_count, tap_count)
    forward_band = banded(taps, width_in, tile_side)
    fields = correlate_forward(extended, forward_band, tile_side)
    doubled = jnp.concatenate([weights, weights])
    partial_sum = jnp.sum(doubled[None, :, None, None] * fields * fields, axis=1)
    intensity = scatter_sum(partial_sum, "kern", 1)
    resist = jax.nn.sigmoid(steepness * (intensity - threshold))
    own_target = lax.dynamic_slice_in_dim(target, kern_place * share_rows, share_rows, 1)
    own_sensitivity = (
        2.0 * (resist - own_target.astype(jnp.float32)) * steepness * resist * (1.0 - resist)
    )
    sensitivity = gather_blocks(own_sensitivity, "kern", 1)
    scaled = (2.0 * doubled)[None, :, None, None] * sensitivity[:, None] * fields
    adjoint_source = scaled.astype(jnp.bfloat16)
    source_strips = jnp.stack(
        [adjoint_source[:, :, :half_width, :], adjoint_source[:, :, tile_side - half_width :, :]]
    )
    source_framed = padded_2(source_strips, (("tile", 0),), 1)
    source_ext = assemble(adjoint_source, source_framed[0], source_framed[3], neighbours)
    adjoint_band = banded(taps[:, ::-1, ::-1], width_in, tile_side)
    gradient_term = correlate_adjoint(source_ext, adjoint_band, tile_side)
    gradient = scatter_sum(gradient_term, "kern", 1)
    return (gradient, resist)


def solution(mesh):
    in_specs = (
        P("tile", None, None),
        P(None, "kern", None, None),
        P("kern"),
        P("tile", None, None),
        P("tile", None),
    )
    out_specs = (P("tile", "kern", None), P("tile", "kern", None))
    return jax.shard_map(shards, mesh=mesh, in_specs=in_specs, out_specs=out_specs, check_vma=False)
```

```python
import jax
import jax.numpy as jnp
from jax import lax
from jax.sharding import PartitionSpec as P

steepness = 8.0
threshold = 0.5


def banded(taps, width_in, width_out):
    tap_count = taps.shape[2]
    shape = (tap_count, width_out, width_in)
    along = lax.broadcasted_iota(jnp.int32, shape, 0)
    row = lax.broadcasted_iota(jnp.int32, shape, 1)
    col = lax.broadcasted_iota(jnp.int32, shape, 2)
    select = (col - row == along).astype(taps.dtype)
    band = jnp.einsum(
        "acb,bji->acji", taps.transpose(1, 0, 2), select, preferred_element_type=jnp.float32
    )
    return band.astype(taps.dtype)


def scatter_sum(value, axis, dim):
    pieces = lax.all_to_all(value, axis, dim, 0, tiled=True)
    return jnp.sum(pieces, axis=0, keepdims=True)


def shifted_rows(images, tap_count, rows_out):
    rows_in = images.shape[-2]
    shape = (tap_count, rows_out, rows_in)
    along = lax.broadcasted_iota(jnp.int32, shape, 0)
    row = lax.broadcasted_iota(jnp.int32, shape, 1)
    source = lax.broadcasted_iota(jnp.int32, shape, 2)
    return (source - row == along).astype(images.dtype)


def correlate_forward(images, band, rows_out):
    select = shifted_rows(images, band.shape[0], rows_out)
    stacked = jnp.einsum(
        "apr,tri->tapi", select, images, preferred_element_type=jnp.float32
    ).astype(images.dtype)
    total = jnp.einsum("tapi,acqi->tcpq", stacked, band, preferred_element_type=jnp.float32)
    return total


def correlate_adjoint(images, band, rows_out):
    select = shifted_rows(images, band.shape[0], rows_out)
    stacked = jnp.einsum(
        "apr,tcri->tacpi", select, images, preferred_element_type=jnp.float32
    ).astype(images.dtype)
    return jnp.einsum("tacpi,acqi->tpq", stacked, band, preferred_element_type=jnp.float32)


def halo_rows(rows, direction):
    devices = lax.axis_size("tile")
    up = [(i, i + 1) for i in range(devices - 1)]
    pairs = up if direction == "up" else [(j, i) for i, j in up]
    return lax.ppermute(rows, "tile", pairs)


def by_block(own, halo, blocks):
    own_rows = own.shape[-2] // blocks
    halo_rows_each = halo.shape[-2] // blocks
    lead = own.shape[:-2]
    own_split = own.reshape(lead + (blocks, own_rows, own.shape[-1]))
    halo_split = halo.reshape(lead + (blocks, halo_rows_each, halo.shape[-1]))
    return jnp.concatenate([own_split, halo_split], axis=-2)


def shards(mask, kernels, weights, target, neighbours):
    tile_side = mask.shape[1]
    local_kernels = kernels.shape[1]
    tap_count = kernels.shape[2]
    half_width = (tap_count - 1) // 2
    reach = 2 * half_width
    kern_count = lax.axis_size("kern")
    kern_place = lax.axis_index("kern")
    share_rows = tile_side // kern_count
    width_in = tile_side + 2 * half_width
    rows_field = tile_side + 2 * half_width

    north_present = (neighbours[:, 1] >= 0).astype(jnp.float32)[:, None, None]
    south_present = (neighbours[:, 6] >= 0).astype(jnp.float32)[:, None, None]
    to_south = jnp.concatenate(
        [mask[:, tile_side - reach :], target[:, tile_side - half_width :]], axis=1
    )
    to_north = jnp.concatenate([mask[:, :reach], target[:, :half_width]], axis=1)
    north_pack = halo_rows(to_south, "up")
    south_pack = halo_rows(to_north, "down")
    north_mask, north_target = north_pack[:, :reach], north_pack[:, reach:]
    south_mask, south_target = south_pack[:, :reach], south_pack[:, reach:]
    north_mask = (north_mask.astype(jnp.float32) * north_present).astype(mask.dtype)
    south_mask = (south_mask.astype(jnp.float32) * south_present).astype(mask.dtype)
    image = jnp.concatenate([north_mask, mask, south_mask], axis=1)
    image = jnp.pad(image, ((0, 0), (0, 0), (half_width, half_width)))

    taps = kernels.reshape(2 * local_kernels, tap_count, tap_count)
    forward_band = banded(taps, width_in, tile_side)
    fields = correlate_forward(image, forward_band, rows_field)
    doubled = jnp.concatenate([weights, weights])
    partial_sum = jnp.sum(doubled[None, :, None, None] * fields * fields, axis=1)[0]

    def own_and_halo(values):
        own = values[..., half_width : half_width + tile_side, :]
        halo = jnp.concatenate(
            [values[..., :half_width, :], values[..., half_width + tile_side :, :]], axis=-2
        )
        return own, halo

    pieces = by_block(*own_and_halo(partial_sum), kern_count)
    intensity = jnp.sum(lax.all_to_all(pieces, "kern", 0, 0, tiled=True), axis=0)
    resist_block = jax.nn.sigmoid(steepness * (intensity - threshold))
    target_rows = jnp.concatenate(
        [north_target[0], target[0], south_target[0]], axis=0
    ).astype(jnp.float32)
    target_pieces = by_block(*own_and_halo(target_rows), kern_count)
    own_target = lax.dynamic_index_in_dim(target_pieces, kern_place, 0, keepdims=False)
    own_sensitivity = (
        2.0
        * (resist_block - own_target)
        * steepness
        * resist_block
        * (1.0 - resist_block)
    )
    copies = jnp.broadcast_to(own_sensitivity, (kern_count,) + own_sensitivity.shape)
    gathered = lax.all_to_all(copies, "kern", 0, 0, tiled=True)
    sens_own = gathered[:, :share_rows].reshape(tile_side, tile_side)
    sens_halo = gathered[:, share_rows:].reshape(2 * half_width, tile_side)
    sens_north = sens_halo[:half_width] * north_present[0]
    sens_south = sens_halo[half_width:] * south_present[0]
    sensitivity = jnp.concatenate([sens_north, sens_own, sens_south], axis=0)
    scaled = (2.0 * doubled)[None, :, None, None] * sensitivity[None, None] * fields
    adjoint_source = scaled.astype(jnp.bfloat16)
    source_ext = jnp.pad(adjoint_source, ((0, 0), (0, 0), (0, 0), (half_width, half_width)))
    adjoint_band = banded(taps[:, ::-1, ::-1], width_in, tile_side)
    gradient_term = correlate_adjoint(source_ext, adjoint_band, tile_side)
    gradient = scatter_sum(gradient_term, "kern", 1)
    resist = resist_block[None, :share_rows]
    return (gradient, resist)


def solution(mesh):
    in_specs = (
        P("tile", None, None),
        P(None, "kern", None, None),
        P("kern"),
        P("tile", None, None),
        P("tile", None),
    )
    out_specs = (P("tile", "kern", None), P("tile", "kern", None))
    return jax.shard_map(shards, mesh=mesh, in_specs=in_specs, out_specs=out_specs, check_vma=False)
```

```python
import jax
import jax.numpy as jnp
from jax import lax
from jax.sharding import PartitionSpec as P

steepness = 8.0
threshold = 0.5


def banded(taps, width_in, width_out):
    tap_count = taps.shape[2]
    shape = (tap_count, width_out, width_in)
    along = lax.broadcasted_iota(jnp.int32, shape, 0)
    row = lax.broadcasted_iota(jnp.int32, shape, 1)
    col = lax.broadcasted_iota(jnp.int32, shape, 2)
    select = (col - row == along).astype(taps.dtype)
    band = jnp.einsum(
        "acb,bji->acji", taps.transpose(1, 0, 2), select, preferred_element_type=jnp.float32
    )
    return band.astype(taps.dtype)


def scatter_sum(value, axis, dim):
    pieces = lax.all_to_all(value, axis, dim, 0, tiled=True)
    return jnp.sum(pieces, axis=0, keepdims=True)


def shifted_rows(images, tap_count, rows_out):
    rows_in = images.shape[-2]
    shape = (tap_count, rows_out, rows_in)
    along = lax.broadcasted_iota(jnp.int32, shape, 0)
    row = lax.broadcasted_iota(jnp.int32, shape, 1)
    source = lax.broadcasted_iota(jnp.int32, shape, 2)
    return (source - row == along).astype(images.dtype)


def correlate_forward(images, band, rows_out):
    select = shifted_rows(images, band.shape[0], rows_out)
    stacked = jnp.einsum(
        "apr,tri->tapi", select, images, preferred_element_type=jnp.float32
    ).astype(images.dtype)
    total = jnp.einsum("tapi,acqi->tcpq", stacked, band, preferred_element_type=jnp.float32)
    return total


def correlate_adjoint(images, band, rows_out):
    select = shifted_rows(images, band.shape[0], rows_out)
    stacked = jnp.einsum(
        "apr,tcri->tacpi", select, images, preferred_element_type=jnp.float32
    ).astype(images.dtype)
    return jnp.einsum("tacpi,acqi->tpq", stacked, band, preferred_element_type=jnp.float32)


def halo_rows(rows, direction):
    devices = lax.axis_size("tile")
    up = [(i, i + 1) for i in range(devices - 1)]
    pairs = up if direction == "up" else [(j, i) for i, j in up]
    return lax.ppermute(rows, "tile", pairs)


def shards(mask, kernels, weights, target, neighbours):
    tile_side = mask.shape[1]
    local_kernels = kernels.shape[1]
    tap_count = kernels.shape[2]
    half_width = (tap_count - 1) // 2
    reach = 2 * half_width
    kern_count = lax.axis_size("kern")
    kern_place = lax.axis_index("kern")
    share_rows = tile_side // kern_count
    width_in = tile_side + 2 * half_width
    rows_field = tile_side + 2 * half_width

    north_present = (neighbours[:, 1] >= 0).astype(jnp.float32)[:, None, None]
    south_present = (neighbours[:, 6] >= 0).astype(jnp.float32)[:, None, None]
    to_south = jnp.concatenate(
        [mask[:, tile_side - reach :], target[:, tile_side - half_width :]], axis=1
    )
    to_north = jnp.concatenate([mask[:, :reach], target[:, :half_width]], axis=1)
    north_pack = halo_rows(to_south, "up")
    south_pack = halo_rows(to_north, "down")
    north_mask, north_target = north_pack[:, :reach], north_pack[:, reach:]
    south_mask, south_target = south_pack[:, :reach], south_pack[:, reach:]
    north_mask = (north_mask.astype(jnp.float32) * north_present).astype(mask.dtype)
    south_mask = (south_mask.astype(jnp.float32) * south_present).astype(mask.dtype)
    image = jnp.concatenate([north_mask, mask, south_mask], axis=1)
    image = jnp.pad(image, ((0, 0), (0, 0), (half_width, half_width)))

    taps = kernels.reshape(2 * local_kernels, tap_count, tap_count)
    forward_band = banded(taps, width_in, tile_side)
    fields = correlate_forward(image, forward_band, rows_field)
    doubled = jnp.concatenate([weights, weights])
    partial_sum = jnp.sum(doubled[None, :, None, None] * fields * fields, axis=1)[0]

    copies = jnp.broadcast_to(partial_sum, (kern_count,) + partial_sum.shape)
    intensity = jnp.sum(lax.all_to_all(copies, "kern", 0, 0, tiled=True), axis=0)
    resist_rows = jax.nn.sigmoid(steepness * (intensity - threshold))
    target_rows = jnp.concatenate(
        [north_target[0], target[0], south_target[0]], axis=0
    ).astype(jnp.float32)
    rows_sensitivity = (
        2.0 * (resist_rows - target_rows) * steepness * resist_rows * (1.0 - resist_rows)
    )
    row_index = lax.broadcasted_iota(jnp.int32, (rows_field, 1), 0)
    present = jnp.where(
        row_index < half_width,
        north_present[0],
        jnp.where(row_index >= half_width + tile_side, south_present[0], 1.0),
    )
    sensitivity = rows_sensitivity * present
    scaled = (2.0 * doubled)[None, :, None, None] * sensitivity[None, None] * fields
    adjoint_source = scaled.astype(jnp.bfloat16)
    source_ext = jnp.pad(adjoint_source, ((0, 0), (0, 0), (0, 0), (half_width, half_width)))
    adjoint_band = banded(taps[:, ::-1, ::-1], width_in, tile_side)
    gradient_term = correlate_adjoint(source_ext, adjoint_band, tile_side)
    gradient = scatter_sum(gradient_term, "kern", 1)
    resist = lax.dynamic_slice_in_dim(
        resist_rows, half_width + kern_place * share_rows, share_rows, 0
    )[None]
    return (gradient, resist)


def solution(mesh):
    in_specs = (
        P("tile", None, None),
        P(None, "kern", None, None),
        P("kern"),
        P("tile", None, None),
        P("tile", None),
    )
    out_specs = (P("tile", "kern", None), P("tile", "kern", None))
    return jax.shard_map(shards, mesh=mesh, in_specs=in_specs, out_specs=out_specs, check_vma=False)
```

```python
import jax
import jax.numpy as jnp
from jax import lax
from jax.sharding import PartitionSpec as P

steepness = 8.0
threshold = 0.5


def banded(taps, width_in, width_out):
    tap_count = taps.shape[2]
    shape = (tap_count, width_out, width_in)
    along = lax.broadcasted_iota(jnp.int32, shape, 0)
    row = lax.broadcasted_iota(jnp.int32, shape, 1)
    col = lax.broadcasted_iota(jnp.int32, shape, 2)
    select = (col - row == along).astype(taps.dtype)
    band = jnp.einsum(
        "acb,bji->acji", taps.transpose(1, 0, 2), select, preferred_element_type=jnp.float32
    )
    return band.astype(taps.dtype)


def scatter_sum(value, axis, dim):
    pieces = lax.all_to_all(value, axis, dim, 0, tiled=True)
    return jnp.sum(pieces, axis=0, keepdims=True)


def shifted_rows(images, tap_count, rows_out):
    rows_in = images.shape[-2]
    shape = (tap_count, rows_out, rows_in)
    along = lax.broadcasted_iota(jnp.int32, shape, 0)
    row = lax.broadcasted_iota(jnp.int32, shape, 1)
    source = lax.broadcasted_iota(jnp.int32, shape, 2)
    return (source - row == along).astype(images.dtype)


def correlate_forward(images, band, rows_out):
    select = shifted_rows(images, band.shape[0], rows_out)
    stacked = jnp.einsum(
        "apr,tri->tapi", select, images, preferred_element_type=jnp.float32
    ).astype(images.dtype)
    total = jnp.einsum("tapi,acqi->tcpq", stacked, band, preferred_element_type=jnp.float32)
    return total


def correlate_adjoint(images, band, rows_out):
    select = shifted_rows(images, band.shape[0], rows_out)
    stacked = jnp.einsum(
        "apr,tcri->tacpi", select, images, preferred_element_type=jnp.float32
    ).astype(images.dtype)
    return jnp.einsum("tacpi,acqi->tpq", stacked, band, preferred_element_type=jnp.float32)


def halo_rows(rows, direction):
    devices = lax.axis_size("tile")
    up = [(i, i + 1) for i in range(devices - 1)]
    pairs = up if direction == "up" else [(j, i) for i, j in up]
    return lax.ppermute(rows, "tile", pairs)


def by_block(own, halo, blocks):
    own_rows = own.shape[-2] // blocks
    halo_rows_each = halo.shape[-2] // blocks
    lead = own.shape[:-2]
    own_split = own.reshape(lead + (blocks, own_rows, own.shape[-1]))
    halo_split = halo.reshape(lead + (blocks, halo_rows_each, halo.shape[-1]))
    return jnp.concatenate([own_split, halo_split], axis=-2)


def shards(mask, kernels, weights, target, neighbours):
    tile_side = mask.shape[1]
    local_kernels = kernels.shape[1]
    tap_count = kernels.shape[2]
    half_width = (tap_count - 1) // 2
    reach = 2 * half_width
    kern_count = lax.axis_size("kern")
    kern_place = lax.axis_index("kern")
    share_rows = tile_side // kern_count
    width_in = tile_side + 2 * half_width
    rows_field = tile_side + 2 * half_width

    north_present = (neighbours[:, 1] >= 0).astype(jnp.float32)[:, None, None]
    south_present = (neighbours[:, 6] >= 0).astype(jnp.float32)[:, None, None]
    to_south = jnp.concatenate(
        [mask[:, tile_side - reach :], target[:, tile_side - half_width :]], axis=1
    )
    to_north = jnp.concatenate([mask[:, :reach], target[:, :half_width]], axis=1)
    north_pack = halo_rows(to_south, "up")
    south_pack = halo_rows(to_north, "down")
    north_mask, north_target = north_pack[:, :reach], north_pack[:, reach:]
    south_mask, south_target = south_pack[:, :reach], south_pack[:, reach:]
    north_mask = (north_mask.astype(jnp.float32) * north_present).astype(mask.dtype)
    south_mask = (south_mask.astype(jnp.float32) * south_present).astype(mask.dtype)
    columns = ((0, 0), (0, 0), (half_width, half_width))
    inner = jnp.pad(mask, columns)
    edges = jnp.pad(
        jnp.concatenate(
            [
                jnp.concatenate([north_mask, mask[:, : tile_side - reach]], axis=1),
                jnp.concatenate([mask[:, reach:], south_mask], axis=1),
            ],
            axis=0,
        ),
        columns,
    )

    taps = kernels.reshape(2 * local_kernels, tap_count, tap_count)
    forward_band = banded(taps, width_in, tile_side)
    inner_rows = tile_side - reach
    middle = correlate_forward(inner, forward_band, inner_rows)
    outer = correlate_forward(edges, forward_band, reach)
    fields = jnp.concatenate([outer[:1], middle, outer[1:]], axis=2)
    doubled = jnp.concatenate([weights, weights])
    partial_sum = jnp.sum(doubled[None, :, None, None] * fields * fields, axis=1)[0]
    flipped, partial_sum = lax.optimization_barrier((taps[:, ::-1, ::-1], partial_sum))

    def own_and_halo(values):
        own = values[..., half_width : half_width + tile_side, :]
        halo = jnp.concatenate(
            [values[..., :half_width, :], values[..., half_width + tile_side :, :]], axis=-2
        )
        return own, halo

    pieces = by_block(*own_and_halo(partial_sum), kern_count)
    intensity = jnp.sum(lax.all_to_all(pieces, "kern", 0, 0, tiled=True), axis=0)
    resist_block = jax.nn.sigmoid(steepness * (intensity - threshold))
    target_rows = jnp.concatenate(
        [north_target[0], target[0], south_target[0]], axis=0
    ).astype(jnp.float32)
    target_pieces = by_block(*own_and_halo(target_rows), kern_count)
    own_target = lax.dynamic_index_in_dim(target_pieces, kern_place, 0, keepdims=False)
    own_sensitivity = (
        2.0
        * (resist_block - own_target)
        * steepness
        * resist_block
        * (1.0 - resist_block)
    )
    copies = jnp.broadcast_to(own_sensitivity, (kern_count,) + own_sensitivity.shape)
    gathered = lax.all_to_all(copies, "kern", 0, 0, tiled=True)
    sens_own = gathered[:, :share_rows].reshape(tile_side, tile_side)
    sens_halo = gathered[:, share_rows:].reshape(2 * half_width, tile_side)
    sens_north = sens_halo[:half_width] * north_present[0]
    sens_south = sens_halo[half_width:] * south_present[0]
    sensitivity = jnp.concatenate([sens_north, sens_own, sens_south], axis=0)
    scaled = (2.0 * doubled)[None, :, None, None] * sensitivity[None, None] * fields
    adjoint_source = scaled.astype(jnp.bfloat16)
    source_ext = jnp.pad(adjoint_source, ((0, 0), (0, 0), (0, 0), (half_width, half_width)))
    adjoint_band = banded(flipped, width_in, tile_side)
    gradient_term = correlate_adjoint(source_ext, adjoint_band, tile_side)
    gradient = scatter_sum(gradient_term, "kern", 1)
    resist = resist_block[None, :share_rows]
    return (gradient, resist)


def solution(mesh):
    in_specs = (
        P("tile", None, None),
        P(None, "kern", None, None),
        P("kern"),
        P("tile", None, None),
        P("tile", None),
    )
    out_specs = (P("tile", "kern", None), P("tile", "kern", None))
    return jax.shard_map(shards, mesh=mesh, in_specs=in_specs, out_specs=out_specs, check_vma=False)
```

```python
import jax
import jax.numpy as jnp
from jax import lax
from jax.sharding import PartitionSpec as P

steepness = 8.0
threshold = 0.5


def banded(taps, width_in, width_out):
    tap_count = taps.shape[2]
    shape = (tap_count, width_out, width_in)
    along = lax.broadcasted_iota(jnp.int32, shape, 0)
    row = lax.broadcasted_iota(jnp.int32, shape, 1)
    col = lax.broadcasted_iota(jnp.int32, shape, 2)
    select = (col - row == along).astype(taps.dtype)
    band = jnp.einsum(
        "acb,bji->acji", taps.transpose(1, 0, 2), select, preferred_element_type=jnp.float32
    )
    return band.astype(taps.dtype)


def scatter_sum(value, axis, dim):
    pieces = lax.all_to_all(value, axis, dim, 0, tiled=True)
    return jnp.sum(pieces, axis=0, keepdims=True)


def shifted_rows(images, tap_count, rows_out):
    rows_in = images.shape[-2]
    shape = (tap_count, rows_out, rows_in)
    along = lax.broadcasted_iota(jnp.int32, shape, 0)
    row = lax.broadcasted_iota(jnp.int32, shape, 1)
    source = lax.broadcasted_iota(jnp.int32, shape, 2)
    return (source - row == along).astype(images.dtype)


def correlate_forward(images, bands, rows_out):
    select = shifted_rows(images, bands[0].shape[0], rows_out)
    stacked = jnp.einsum(
        "apr,tri->tapi", select, images, preferred_element_type=jnp.float32
    ).astype(images.dtype)
    per_channel = [
        jnp.einsum("tapi,aqi->tpq", stacked, band, preferred_element_type=jnp.float32)
        for band in bands
    ]
    return jnp.stack(per_channel, axis=1)


def correlate_adjoint(images, band, rows_out):
    select = shifted_rows(images, band.shape[0], rows_out)
    stacked = jnp.einsum(
        "apr,tcri->tacpi", select, images, preferred_element_type=jnp.float32
    ).astype(images.dtype)
    return jnp.einsum("tacpi,acqi->tpq", stacked, band, preferred_element_type=jnp.float32)


def halo_rows(rows, direction):
    devices = lax.axis_size("tile")
    up = [(i, i + 1) for i in range(devices - 1)]
    pairs = up if direction == "up" else [(j, i) for i, j in up]
    return lax.ppermute(rows, "tile", pairs)


def by_block(own, halo, blocks):
    own_rows = own.shape[-2] // blocks
    halo_rows_each = halo.shape[-2] // blocks
    lead = own.shape[:-2]
    own_split = own.reshape(lead + (blocks, own_rows, own.shape[-1]))
    halo_split = halo.reshape(lead + (blocks, halo_rows_each, halo.shape[-1]))
    return jnp.concatenate([own_split, halo_split], axis=-2)


def shards(mask, kernels, weights, target, neighbours):
    tile_side = mask.shape[1]
    local_kernels = kernels.shape[1]
    tap_count = kernels.shape[2]
    half_width = (tap_count - 1) // 2
    reach = 2 * half_width
    kern_count = lax.axis_size("kern")
    kern_place = lax.axis_index("kern")
    share_rows = tile_side // kern_count
    width_in = tile_side + 2 * half_width
    rows_field = tile_side + 2 * half_width

    north_present = (neighbours[:, 1] >= 0).astype(jnp.float32)[:, None, None]
    south_present = (neighbours[:, 6] >= 0).astype(jnp.float32)[:, None, None]
    to_south = jnp.concatenate(
        [mask[:, tile_side - reach :], target[:, tile_side - half_width :]], axis=1
    )
    to_north = jnp.concatenate([mask[:, :reach], target[:, :half_width]], axis=1)
    north_pack = halo_rows(to_south, "up")
    south_pack = halo_rows(to_north, "down")
    north_mask, north_target = north_pack[:, :reach], north_pack[:, reach:]
    south_mask, south_target = south_pack[:, :reach], south_pack[:, reach:]
    north_mask = (north_mask.astype(jnp.float32) * north_present).astype(mask.dtype)
    south_mask = (south_mask.astype(jnp.float32) * south_present).astype(mask.dtype)
    columns = ((0, 0), (0, 0), (half_width, half_width))
    inner = jnp.pad(mask, columns)
    edges = jnp.pad(
        jnp.concatenate(
            [
                jnp.concatenate([north_mask, mask[:, : tile_side - reach]], axis=1),
                jnp.concatenate([mask[:, reach:], south_mask], axis=1),
            ],
            axis=0,
        ),
        columns,
    )

    taps = kernels.reshape(2 * local_kernels, tap_count, tap_count)
    forward_band = [
        banded(taps[c : c + 1], width_in, tile_side)[:, 0] for c in range(taps.shape[0])
    ]
    inner_rows = tile_side - reach
    middle = correlate_forward(inner, forward_band, inner_rows)
    outer = correlate_forward(edges, forward_band, reach)
    fields = jnp.concatenate([outer[:1], middle, outer[1:]], axis=2)
    doubled = jnp.concatenate([weights, weights])
    partial_sum = jnp.sum(doubled[None, :, None, None] * fields * fields, axis=1)[0]
    flipped, partial_sum = lax.optimization_barrier((taps[:, ::-1, ::-1], partial_sum))

    def own_and_halo(values):
        own = values[..., half_width : half_width + tile_side, :]
        halo = jnp.concatenate(
            [values[..., :half_width, :], values[..., half_width + tile_side :, :]], axis=-2
        )
        return own, halo

    pieces = by_block(*own_and_halo(partial_sum), kern_count)
    intensity = jnp.sum(lax.all_to_all(pieces, "kern", 0, 0, tiled=True), axis=0)
    resist_block = jax.nn.sigmoid(steepness * (intensity - threshold))
    target_rows = jnp.concatenate(
        [north_target[0], target[0], south_target[0]], axis=0
    ).astype(jnp.float32)
    target_pieces = by_block(*own_and_halo(target_rows), kern_count)
    own_target = lax.dynamic_index_in_dim(target_pieces, kern_place, 0, keepdims=False)
    own_sensitivity = (
        2.0
        * (resist_block - own_target)
        * steepness
        * resist_block
        * (1.0 - resist_block)
    )
    copies = jnp.broadcast_to(own_sensitivity, (kern_count,) + own_sensitivity.shape)
    gathered = lax.all_to_all(copies, "kern", 0, 0, tiled=True)
    sens_own = gathered[:, :share_rows].reshape(tile_side, tile_side)
    sens_halo = gathered[:, share_rows:].reshape(2 * half_width, tile_side)
    sens_north = sens_halo[:half_width] * north_present[0]
    sens_south = sens_halo[half_width:] * south_present[0]
    sensitivity = jnp.concatenate([sens_north, sens_own, sens_south], axis=0)
    scaled = (2.0 * doubled)[None, :, None, None] * sensitivity[None, None] * fields
    adjoint_source = scaled.astype(jnp.bfloat16)
    source_ext = jnp.pad(adjoint_source, ((0, 0), (0, 0), (0, 0), (half_width, half_width)))
    adjoint_band = banded(flipped, width_in, tile_side)
    gradient_term = correlate_adjoint(source_ext, adjoint_band, tile_side)
    gradient = scatter_sum(gradient_term, "kern", 1)
    resist = resist_block[None, :share_rows]
    return (gradient, resist)


def solution(mesh):
    in_specs = (
        P("tile", None, None),
        P(None, "kern", None, None),
        P("kern"),
        P("tile", None, None),
        P("tile", None),
    )
    out_specs = (P("tile", "kern", None), P("tile", "kern", None))
    return jax.shard_map(shards, mesh=mesh, in_specs=in_specs, out_specs=out_specs, check_vma=False)
```

```python
import jax
import jax.numpy as jnp
from jax import lax
from jax.sharding import PartitionSpec as P

steepness = 8.0
threshold = 0.5


def banded(taps, width_in, width_out):
    tap_count = taps.shape[2]
    shape = (tap_count, width_out, width_in)
    along = lax.broadcasted_iota(jnp.int32, shape, 0)
    row = lax.broadcasted_iota(jnp.int32, shape, 1)
    col = lax.broadcasted_iota(jnp.int32, shape, 2)
    select = (col - row == along).astype(taps.dtype)
    band = jnp.einsum(
        "acb,bji->acji", taps.transpose(1, 0, 2), select, preferred_element_type=jnp.float32
    )
    return band.astype(taps.dtype)


def scatter_sum(value, axis, dim):
    pieces = lax.all_to_all(value, axis, dim, 0, tiled=True)
    return jnp.sum(pieces, axis=0, keepdims=True)


def shifted_rows(images, tap_count, rows_out):
    rows_in = images.shape[-2]
    shape = (tap_count, rows_out, rows_in)
    along = lax.broadcasted_iota(jnp.int32, shape, 0)
    row = lax.broadcasted_iota(jnp.int32, shape, 1)
    source = lax.broadcasted_iota(jnp.int32, shape, 2)
    return (source - row == along).astype(images.dtype)


def correlate_forward(images, bands, rows_out):
    select = shifted_rows(images, bands[0].shape[0], rows_out)
    stacked = jnp.einsum(
        "apr,tri->tapi", select, images, preferred_element_type=jnp.float32
    ).astype(images.dtype)
    per_channel = [
        jnp.einsum("tapi,aqi->tpq", stacked, band, preferred_element_type=jnp.float32)
        for band in bands
    ]
    return jnp.stack(per_channel, axis=1)


def correlate_adjoint(images, bands, rows_out):
    select = shifted_rows(images, bands[0].shape[0], rows_out)
    total = None
    for channel, band in enumerate(bands):
        stacked = jnp.einsum(
            "apr,tri->tapi", select, images[:, channel], preferred_element_type=jnp.float32
        ).astype(images.dtype)
        term = jnp.einsum("tapi,aqi->tpq", stacked, band, preferred_element_type=jnp.float32)
        total = term if total is None else total + term
    return total


def halo_rows(rows, direction):
    devices = lax.axis_size("tile")
    up = [(i, i + 1) for i in range(devices - 1)]
    pairs = up if direction == "up" else [(j, i) for i, j in up]
    return lax.ppermute(rows, "tile", pairs)


def by_block(own, halo, blocks):
    own_rows = own.shape[-2] // blocks
    halo_rows_each = halo.shape[-2] // blocks
    lead = own.shape[:-2]
    own_split = own.reshape(lead + (blocks, own_rows, own.shape[-1]))
    halo_split = halo.reshape(lead + (blocks, halo_rows_each, halo.shape[-1]))
    return jnp.concatenate([own_split, halo_split], axis=-2)


def shards(mask, kernels, weights, target, neighbours):
    tile_side = mask.shape[1]
    local_kernels = kernels.shape[1]
    tap_count = kernels.shape[2]
    half_width = (tap_count - 1) // 2
    reach = 2 * half_width
    kern_count = lax.axis_size("kern")
    kern_place = lax.axis_index("kern")
    share_rows = tile_side // kern_count
    width_in = tile_side + 2 * half_width
    rows_field = tile_side + 2 * half_width

    north_present = (neighbours[:, 1] >= 0).astype(jnp.float32)[:, None, None]
    south_present = (neighbours[:, 6] >= 0).astype(jnp.float32)[:, None, None]
    to_south = jnp.concatenate(
        [mask[:, tile_side - reach :], target[:, tile_side - half_width :]], axis=1
    )
    to_north = jnp.concatenate([mask[:, :reach], target[:, :half_width]], axis=1)
    north_pack = halo_rows(to_south, "up")
    south_pack = halo_rows(to_north, "down")
    north_mask, north_target = north_pack[:, :reach], north_pack[:, reach:]
    south_mask, south_target = south_pack[:, :reach], south_pack[:, reach:]
    north_mask = (north_mask.astype(jnp.float32) * north_present).astype(mask.dtype)
    south_mask = (south_mask.astype(jnp.float32) * south_present).astype(mask.dtype)
    columns = ((0, 0), (0, 0), (half_width, half_width))
    inner = jnp.pad(mask, columns)
    edges = jnp.pad(
        jnp.concatenate(
            [
                jnp.concatenate([north_mask, mask[:, : tile_side - reach]], axis=1),
                jnp.concatenate([mask[:, reach:], south_mask], axis=1),
            ],
            axis=0,
        ),
        columns,
    )

    taps = kernels.reshape(2 * local_kernels, tap_count, tap_count)
    forward_band = [
        banded(taps[c : c + 1], width_in, tile_side)[:, 0] for c in range(taps.shape[0])
    ]
    inner_rows = tile_side - reach
    middle = correlate_forward(inner, forward_band, inner_rows)
    outer = correlate_forward(edges, forward_band, reach)
    fields = jnp.concatenate([outer[:1], middle, outer[1:]], axis=2)
    doubled = jnp.concatenate([weights, weights])
    partial_sum = jnp.sum(doubled[None, :, None, None] * fields * fields, axis=1)[0]
    flipped, partial_sum = lax.optimization_barrier((taps[:, ::-1, ::-1], partial_sum))

    def own_and_halo(values):
        own = values[..., half_width : half_width + tile_side, :]
        halo = jnp.concatenate(
            [values[..., :half_width, :], values[..., half_width + tile_side :, :]], axis=-2
        )
        return own, halo

    pieces = by_block(*own_and_halo(partial_sum), kern_count)
    intensity = jnp.sum(lax.all_to_all(pieces, "kern", 0, 0, tiled=True), axis=0)
    resist_block = jax.nn.sigmoid(steepness * (intensity - threshold))
    target_rows = jnp.concatenate(
        [north_target[0], target[0], south_target[0]], axis=0
    ).astype(jnp.float32)
    target_pieces = by_block(*own_and_halo(target_rows), kern_count)
    own_target = lax.dynamic_index_in_dim(target_pieces, kern_place, 0, keepdims=False)
    own_sensitivity = (
        2.0
        * (resist_block - own_target)
        * steepness
        * resist_block
        * (1.0 - resist_block)
    )
    copies = jnp.broadcast_to(own_sensitivity, (kern_count,) + own_sensitivity.shape)
    gathered = lax.all_to_all(copies, "kern", 0, 0, tiled=True)
    sens_own = gathered[:, :share_rows].reshape(tile_side, tile_side)
    sens_halo = gathered[:, share_rows:].reshape(2 * half_width, tile_side)
    sens_north = sens_halo[:half_width] * north_present[0]
    sens_south = sens_halo[half_width:] * south_present[0]
    sensitivity = jnp.concatenate([sens_north, sens_own, sens_south], axis=0)
    scaled = (2.0 * doubled)[None, :, None, None] * sensitivity[None, None] * fields
    adjoint_source = scaled.astype(jnp.bfloat16)
    source_ext = jnp.pad(adjoint_source, ((0, 0), (0, 0), (0, 0), (half_width, half_width)))
    adjoint_band = [
        banded(flipped[c : c + 1], width_in, tile_side)[:, 0] for c in range(flipped.shape[0])
    ]
    gradient_term = correlate_adjoint(source_ext, adjoint_band, tile_side)
    gradient = scatter_sum(gradient_term, "kern", 1)
    resist = resist_block[None, :share_rows]
    return (gradient, resist)


def solution(mesh):
    in_specs = (
        P("tile", None, None),
        P(None, "kern", None, None),
        P("kern"),
        P("tile", None, None),
        P("tile", None),
    )
    out_specs = (P("tile", "kern", None), P("tile", "kern", None))
    return jax.shard_map(shards, mesh=mesh, in_specs=in_specs, out_specs=out_specs, check_vma=False)
```

```python
import jax
import jax.numpy as jnp
from jax import lax
from jax.sharding import PartitionSpec as P

steepness = 8.0
threshold = 0.5


def banded(taps, width_in, width_out):
    tap_count = taps.shape[2]
    shape = (tap_count, width_out, width_in)
    along = lax.broadcasted_iota(jnp.int32, shape, 0)
    row = lax.broadcasted_iota(jnp.int32, shape, 1)
    col = lax.broadcasted_iota(jnp.int32, shape, 2)
    select = (col - row == along).astype(taps.dtype)
    band = jnp.einsum(
        "acb,bji->acji", taps.transpose(1, 0, 2), select, preferred_element_type=jnp.float32
    )
    return band.astype(taps.dtype)


def scatter_sum(value, axis, dim):
    pieces = lax.all_to_all(value, axis, dim, 0, tiled=True)
    return jnp.sum(pieces, axis=0, keepdims=True)


def shifted_rows(images, tap_count, rows_out):
    rows_in = images.shape[-2]
    shape = (tap_count, rows_out, rows_in)
    along = lax.broadcasted_iota(jnp.int32, shape, 0)
    row = lax.broadcasted_iota(jnp.int32, shape, 1)
    source = lax.broadcasted_iota(jnp.int32, shape, 2)
    return (source - row == along).astype(images.dtype)


def correlate_forward(images, bands, rows_out):
    select = shifted_rows(images, bands[0].shape[0], rows_out)
    stacked = jnp.einsum(
        "apr,tri->tapi", select, images, preferred_element_type=jnp.float32
    ).astype(images.dtype)
    per_channel = [
        jnp.einsum("tapi,aqi->tpq", stacked, band, preferred_element_type=jnp.float32)
        for band in bands
    ]
    return jnp.stack(per_channel, axis=1)


def correlate_adjoint(images, band, rows_out):
    select = shifted_rows(images, band.shape[0], rows_out)
    stacked = jnp.einsum(
        "apr,tcri->tacpi", select, images, preferred_element_type=jnp.float32
    ).astype(images.dtype)
    return jnp.einsum("tacpi,acqi->tpq", stacked, band, preferred_element_type=jnp.float32)


def halo_rows(rows, direction):
    devices = lax.axis_size("tile")
    up = [(i, i + 1) for i in range(devices - 1)]
    pairs = up if direction == "up" else [(j, i) for i, j in up]
    return lax.ppermute(rows, "tile", pairs)


def by_block(own, halo, blocks):
    own_rows = own.shape[-2] // blocks
    halo_rows_each = halo.shape[-2] // blocks
    lead = own.shape[:-2]
    own_split = own.reshape(lead + (blocks, own_rows, own.shape[-1]))
    halo_split = halo.reshape(lead + (blocks, halo_rows_each, halo.shape[-1]))
    return jnp.concatenate([own_split, halo_split], axis=-2)


def shards(mask, kernels, weights, target, neighbours):
    tile_side = mask.shape[1]
    local_kernels = kernels.shape[1]
    tap_count = kernels.shape[2]
    half_width = (tap_count - 1) // 2
    reach = 2 * half_width
    kern_count = lax.axis_size("kern")
    kern_place = lax.axis_index("kern")
    share_rows = tile_side // kern_count
    width_in = tile_side + 2 * half_width
    rows_field = tile_side + 2 * half_width

    north_present = (neighbours[:, 1] >= 0).astype(jnp.float32)[:, None, None]
    south_present = (neighbours[:, 6] >= 0).astype(jnp.float32)[:, None, None]
    to_south = jnp.concatenate(
        [mask[:, tile_side - reach :], target[:, tile_side - half_width :]], axis=1
    )
    to_north = jnp.concatenate([mask[:, :reach], target[:, :half_width]], axis=1)
    north_pack = halo_rows(to_south, "up")
    south_pack = halo_rows(to_north, "down")
    north_mask, north_target = north_pack[:, :reach], north_pack[:, reach:]
    south_mask, south_target = south_pack[:, :reach], south_pack[:, reach:]
    north_mask = (north_mask.astype(jnp.float32) * north_present).astype(mask.dtype)
    south_mask = (south_mask.astype(jnp.float32) * south_present).astype(mask.dtype)
    columns = ((0, 0), (0, 0), (half_width, half_width))
    inner = jnp.pad(mask, columns)
    edges = jnp.pad(
        jnp.concatenate(
            [
                jnp.concatenate([north_mask, mask[:, : tile_side - reach]], axis=1),
                jnp.concatenate([mask[:, reach:], south_mask], axis=1),
            ],
            axis=0,
        ),
        columns,
    )

    taps = kernels.reshape(2 * local_kernels, tap_count, tap_count)
    forward_band = [
        banded(taps[c : c + 1], width_in, tile_side)[:, 0] for c in range(taps.shape[0])
    ]
    inner_rows = tile_side - reach
    middle = correlate_forward(inner, forward_band, inner_rows)
    outer = correlate_forward(edges, forward_band, reach)
    fields = jnp.concatenate([outer[:1], middle, outer[1:]], axis=2)
    doubled = jnp.concatenate([weights, weights])
    partial_sum = jnp.sum(doubled[None, :, None, None] * fields * fields, axis=1)[0]
    flipped, partial_sum = lax.optimization_barrier((taps[:, ::-1, ::-1], partial_sum))

    def own_and_halo(values):
        own = values[..., half_width : half_width + tile_side, :]
        halo = jnp.concatenate(
            [values[..., :half_width, :], values[..., half_width + tile_side :, :]], axis=-2
        )
        return own, halo

    pieces = by_block(*own_and_halo(partial_sum), kern_count)
    intensity = jnp.sum(lax.all_to_all(pieces, "kern", 0, 0, tiled=True), axis=0)
    resist_block = jax.nn.sigmoid(steepness * (intensity - threshold))
    target_rows = jnp.concatenate(
        [north_target[0], target[0], south_target[0]], axis=0
    ).astype(jnp.float32)
    target_pieces = by_block(*own_and_halo(target_rows), kern_count)
    own_target = lax.dynamic_index_in_dim(target_pieces, kern_place, 0, keepdims=False)
    own_sensitivity = (
        2.0
        * (resist_block - own_target)
        * steepness
        * resist_block
        * (1.0 - resist_block)
    )
    adjoint_band = banded(flipped, width_in, tile_side)
    adjoint_band, own_sensitivity = lax.optimization_barrier((adjoint_band, own_sensitivity))
    copies = jnp.broadcast_to(own_sensitivity, (kern_count,) + own_sensitivity.shape)
    gathered = lax.all_to_all(copies, "kern", 0, 0, tiled=True)
    sens_own = gathered[:, :share_rows].reshape(tile_side, tile_side)
    sens_halo = gathered[:, share_rows:].reshape(2 * half_width, tile_side)
    sens_north = sens_halo[:half_width] * north_present[0]
    sens_south = sens_halo[half_width:] * south_present[0]
    sensitivity = jnp.concatenate([sens_north, sens_own, sens_south], axis=0)
    scaled = (2.0 * doubled)[None, :, None, None] * sensitivity[None, None] * fields
    adjoint_source = scaled.astype(jnp.bfloat16)
    source_ext = jnp.pad(adjoint_source, ((0, 0), (0, 0), (0, 0), (half_width, half_width)))
    gradient_term = correlate_adjoint(source_ext, adjoint_band, tile_side)
    gradient = scatter_sum(gradient_term, "kern", 1)
    resist = resist_block[None, :share_rows]
    return (gradient, resist)


def solution(mesh):
    in_specs = (
        P("tile", None, None),
        P(None, "kern", None, None),
        P("kern"),
        P("tile", None, None),
        P("tile", None),
    )
    out_specs = (P("tile", "kern", None), P("tile", "kern", None))
    return jax.shard_map(shards, mesh=mesh, in_specs=in_specs, out_specs=out_specs, check_vma=False)
```
